256 devices in a mesh: dp: 16 (over z_lo, x), block: 16 (over z_hi, y, core).
Axes of the slice: x: 4, y: 4, z: 8 (z_hi: 2, z_lo: 4; z = z_hi * 4 + z_lo), core: 2. Of those that a mesh axis runs over, the one named last changes fastest.
Arguments:
- inputs: bfloat16 [6144, 8192], P('dp', 'block'), may hold values from -6 to 6
- weight_in: bfloat16 [512, 5, 16384], P('dp', None, 'block'), may hold values from -0.125 to 0.125
- weight_out: bfloat16 [1024, 5, 8192], P('dp', None, 'block'), may hold values from -0.078125 to 0.078125
- cotangent: bfloat16 [6144, 8192], P('dp', 'block'), may hold values from -6 to 6
Outputs:
- outputs: bfloat16 [6144, 8192], P('dp', 'block')
- input_grad: bfloat16 [6144, 8192], P('dp', 'block')
- grad_in: float32 [512, 5, 16384], P('dp', None, 'block')
- grad_out: float32 [1024, 5, 8192], P('dp', None, 'block')
The draws below stay inside these ranges and needn't reach their ends.
All inputs are finite; a program needn't handle non-finite values.
Results may differ from the reference program's by a relative error of at most 0.017.
Values may be sent and summed in bfloat16 or wider, within the bound.
No kernel may reach another device: no remote copies, remote signals or barrier semaphores. Data moves between devices by JAX's collectives and lax.ppermute only.
A program may use at most 128 MiB of HBM per device.

```python
import jax
import jax.numpy as jnp
from jax import lax

BW = 512
HP = 1024
TOK_DEV = 384
LEVELS = 4
D = 8192
H = 16384
TOKENS = 6144
N_DP = 16
N_BLOCK = 16


def shard_levels(stream_key, shape, cuts, least, high):
    def one(position, parts):
        heights = jax.random.uniform(jax.random.fold_in(jax.random.fold_in(stream_key, 6), position), (parts,), jnp.float32, least / len(cuts), high / len(cuts))
        return jnp.repeat(jnp.exp(heights), shape[position] // parts).reshape((-1,) + (1,) * (len(shape) - position - 1))

    loudness = one(*cuts[0])
    for cut in cuts[1:]:
        loudness = loudness * one(*cut)
    return loudness


def noise(key, dims, deviation, bound, pieces=(), dtype=jnp.bfloat16):
    entries = deviation * jax.random.normal(key, dims, jnp.float32)
    if pieces:
        entries = entries * shard_levels(key, dims, pieces, -0.22, 0.18)
    return jnp.clip(entries, -bound, bound).astype(dtype)


def setup_inputs(seed: int = 0) -> dict:
    arg_keys = jax.random.split(jax.random.key(seed), 5)
    return {
        "inputs": noise(arg_keys[0], (TOKENS, D), 1.0, 6.0, ((0, 16), (1, 16))),
        "weight_in": noise(arg_keys[1], (BW, LEVELS + 1, H), (BW * (LEVELS + 1)) ** -0.5, 0.125, ((0, 16), (2, 16))),
        "weight_out": noise(arg_keys[2], (HP, LEVELS + 1, D), (HP * (LEVELS + 1)) ** -0.5, 0.078125, ((0, 16), (2, 16))),
        "cotangent": noise(arg_keys[3], (TOKENS, D), 1.0, 6.0, ((0, 16), (1, 16))),
    }


def distance(level):
    return 0 if level == 0 else 1 << level - 1

def cut(array, index, width):
    return array[:, index * width:(index + 1) * width]

def rounded(value):
    return lax.optimization_barrier(value.astype(jnp.bfloat16)).astype(jnp.float32)

def gelu_tanh(value):
    return jax.nn.gelu(value, approximate=True)

def token_sum(left, right):
    left_rows = left.reshape(N_DP, TOK_DEV, left.shape[1]).astype(jnp.float32)
    right_rows = right.reshape(N_DP, TOK_DEV, right.shape[1]).astype(jnp.float32)
    partial_sums = jnp.einsum('rta,rtb->rab', left_rows, right_rows, precision=lax.Precision.HIGHEST)
    return lax.optimization_barrier(jnp.sum(rounded(partial_sums), axis=0))

def reference(inputs, weight_in, weight_out, cotangent):
    hid_grads = []
    for panel in range(N_BLOCK):
        total = jnp.zeros((TOKENS, HP), jnp.float32)
        for level in range(LEVELS + 1):
            source = panel ^ distance(level)
            term = jnp.dot(cut(cotangent, source, BW), cut(weight_out[:, level, :], source, BW).T, preferred_element_type=jnp.float32)
            total = total + rounded(term)
        hid_grads.append(total)
    hiddens = []
    pre_grads = []
    for panel in range(N_BLOCK):
        pre_act = jnp.zeros((TOKENS, HP), jnp.float32)
        for level in range(LEVELS + 1):
            source = panel ^ distance(level)
            pre_act = pre_act + jnp.dot(cut(inputs, source, BW), cut(weight_in[:, level, :], panel, HP), preferred_element_type=jnp.float32)
        hiddens.append(gelu_tanh(pre_act).astype(jnp.bfloat16))
        slope = jax.vjp(gelu_tanh, pre_act)[1](hid_grads[panel])[0]
        pre_grads.append(slope.astype(jnp.bfloat16))
    out_blocks = []
    grad_blocks = []
    for block in range(N_BLOCK):
        total = jnp.zeros((TOKENS, BW), jnp.float32)
        back = jnp.zeros((TOKENS, BW), jnp.float32)
        for level in range(LEVELS + 1):
            source = block ^ distance(level)
            total = total + jnp.dot(hiddens[source], cut(weight_out[:, level, :], block, BW), preferred_element_type=jnp.float32)
            term = jnp.dot(pre_grads[source], cut(weight_in[:, level, :], source, HP).T, preferred_element_type=jnp.float32)
            back = back + rounded(term)
        out_blocks.append(total.astype(jnp.bfloat16))
        grad_blocks.append(back.astype(jnp.bfloat16))
    outputs = jnp.concatenate(out_blocks, axis=1)
    input_grad = jnp.concatenate(grad_blocks, axis=1)
    in_levels = []
    out_levels = []
    for level in range(LEVELS + 1):
        in_levels.append(jnp.concatenate([token_sum(cut(inputs, panel ^ distance(level), BW), pre_grads[panel]) for panel in range(N_BLOCK)], axis=1))
        out_levels.append(jnp.concatenate([token_sum(hiddens[block ^ distance(level)], cut(cotangent, block, BW)) for block in range(N_BLOCK)], axis=1))
    grad_in = jnp.stack(in_levels, axis=1)
    grad_out = jnp.stack(out_levels, axis=1)
    return (outputs, input_grad, grad_in, grad_out)
```

```python
import jax
import jax.numpy as jnp
from jax import lax
from jax.sharding import PartitionSpec as P


def swapped(value, axis, distance):
    mask = 2**distance
    pairs = [(source, source ^ mask) for source in range(lax.axis_size(axis))]
    return lax.ppermute(value, axis, pairs)


def gelu_tanh(value):
    return jax.nn.gelu(value, approximate=True)


def rounded(value):
    return lax.optimization_barrier(value.astype(jnp.bfloat16)).astype(jnp.float32)


def snake_ring(n_dp):
    xs = 4 if n_dp % 4 == 0 else n_dp
    zs = n_dp // xs
    order = []
    for x in range(xs):
        column = range(zs) if x % 2 == 0 else reversed(range(zs))
        for z in column:
            order.append(z * xs + x)
    return order


def ring_tables(n):
    ring = snake_ring(n)
    pos = [0] * n
    for p, d in enumerate(ring):
        pos[d] = p
    return ring, pos


def ring_shift(value, ring, shift):
    n = len(ring)
    pairs = [(ring[p], ring[(p + shift) % n]) for p in range(n)]
    return lax.ppermute(value, "dp", pairs)


def ring_all_gather(shard):
    n = lax.axis_size("dp")
    ring, pos_of = ring_tables(n)
    ring_arr = jnp.asarray(ring, jnp.int32)
    me = lax.axis_index("dp")
    pos = jnp.asarray(pos_of, jnp.int32)[me]
    out = jnp.zeros((n,) + shard.shape, shard.dtype)
    out = lax.dynamic_update_index_in_dim(out, shard, me, 0)
    cw = shard
    ccw = shard
    half_steps = n // 2
    rows = shard.shape[0]
    for step in range(1, half_steps + 1):
        if step < half_steps:
            cw = ring_shift(cw, ring, 1)
            out = lax.dynamic_update_index_in_dim(out, cw, ring_arr[(pos - step) % n], 0)
            ccw = ring_shift(ccw, ring, -1)
            out = lax.dynamic_update_index_in_dim(out, ccw, ring_arr[(pos + step) % n], 0)
        else:
            first = ring_shift(cw[: rows // 2], ring, 1)
            second = ring_shift(ccw[rows // 2 :], ring, -1)
            piece = jnp.concatenate([first, second], axis=0)
            out = lax.dynamic_update_index_in_dim(out, piece, ring_arr[(pos + step) % n], 0)
    return out.reshape((n * rows,) + shard.shape[1:])


def ring_reduce_scatter(chunks):
    n = lax.axis_size("dp")
    ring, pos_of = ring_tables(n)
    ring_arr = jnp.asarray(ring, jnp.int32)
    me = lax.axis_index("dp")
    pos = jnp.asarray(pos_of, jnp.int32)[me]

    def own(q):
        return lax.dynamic_index_in_dim(chunks, ring_arr[q % n], 0, keepdims=False).astype(jnp.float32)

    cw_steps = n // 2 - 1
    ccw_steps = n // 2
    cw = None
    ccw = None
    for t in range(ccw_steps):
        if t < cw_steps:
            q = pos + cw_steps - t
            acc = own(q) if cw is None else cw.astype(jnp.float32) + own(q)
            cw = ring_shift(acc.astype(jnp.bfloat16), ring, 1)
        q = pos - ccw_steps + t
        acc = own(q) if ccw is None else ccw.astype(jnp.float32) + own(q)
        ccw = ring_shift(acc.astype(jnp.bfloat16), ring, -1)
    return cw.astype(jnp.float32) + ccw.astype(jnp.float32) + own(pos)


def body(inputs, weight_in, weight_out, cotangent):
    levels = lax.axis_size("block").bit_length() - 1
    n_dp = lax.axis_size("dp")
    weight_in_all = ring_all_gather(weight_in)
    weight_out_all = ring_all_gather(weight_out)
    pieces = [inputs]
    for level_bit in range(levels):
        pieces.append(swapped(inputs, "block", level_bit))
    in_stack = jnp.stack(pieces, axis=1)
    pre_act = jnp.einsum("tkc,ckh->th", in_stack, weight_in_all, preferred_element_type=jnp.float32)
    hidden = gelu_tanh(pre_act).astype(jnp.bfloat16)
    hid_pieces = [hidden]
    for level_bit in range(levels):
        hid_pieces.append(swapped(hidden, "block", level_bit))
    hid_stack = jnp.stack(hid_pieces, axis=1)
    outputs = jnp.einsum(
        "tkh,hkc->tc", hid_stack, weight_out_all, preferred_element_type=jnp.float32
    ).astype(jnp.bfloat16)
    grad_out_terms = jnp.einsum("tkh,tc->hkc", hid_stack, cotangent, preferred_element_type=jnp.float32)
    grad_out = ring_reduce_scatter(
        grad_out_terms.astype(jnp.bfloat16).reshape((n_dp, weight_out.shape[0]) + grad_out_terms.shape[1:])
    )
    back_terms = jnp.einsum(
        "tc,hkc->tkh", cotangent, weight_out_all, preferred_element_type=jnp.float32
    )
    back_round = back_terms.astype(jnp.bfloat16)
    hid_grad = rounded(back_terms[:, 0, :])
    for level_bit in range(levels):
        arrived = swapped(back_round[:, level_bit + 1, :], "block", level_bit)
        hid_grad = hid_grad + arrived.astype(jnp.float32)
    slope = jax.vjp(gelu_tanh, pre_act)[1](hid_grad)[0]
    pre_grad = slope.astype(jnp.bfloat16)
    in_terms = jnp.einsum(
        "th,ckh->tkc", pre_grad, weight_in_all, preferred_element_type=jnp.float32
    )
    in_round = in_terms.astype(jnp.bfloat16)
    in_total = rounded(in_terms[:, 0, :])
    for level_bit in range(levels):
        arrived = swapped(in_round[:, level_bit + 1, :], "block", level_bit)
        in_total = in_total + arrived.astype(jnp.float32)
    input_grad = in_total.astype(jnp.bfloat16)
    grad_in_terms = jnp.einsum("tkc,th->ckh", in_stack, pre_grad, preferred_element_type=jnp.float32)
    grad_in = ring_reduce_scatter(
        grad_in_terms.astype(jnp.bfloat16).reshape((n_dp, weight_in.shape[0]) + grad_in_terms.shape[1:])
    )
    return (outputs, input_grad, grad_in, grad_out)


def solution(mesh):
    placed = (P("dp", "block"), P("dp", None, "block"), P("dp", None, "block"), P("dp", "block"))
    return jax.shard_map(
        body,
        mesh=mesh,
        in_specs=placed,
        out_specs=(
            P("dp", "block"),
            P("dp", "block"),
            P("dp", None, "block"),
            P("dp", None, "block"),
        ),
        check_vma=False,
    )
```

```python
import jax
import jax.numpy as jnp
from jax import lax
from jax.sharding import PartitionSpec as P


def swapped(value, axis, distance):
    mask = 2**distance
    pairs = [(source, source ^ mask) for source in range(lax.axis_size(axis))]
    return lax.ppermute(value, axis, pairs)


def gelu_tanh(value):
    return jax.nn.gelu(value, approximate=True)


def rounded(value):
    return lax.optimization_barrier(value.astype(jnp.bfloat16)).astype(jnp.float32)


def snake_ring(n_dp):
    xs = 4 if n_dp % 4 == 0 else n_dp
    zs = n_dp // xs
    order = []
    for x in range(xs):
        column = range(zs) if x % 2 == 0 else reversed(range(zs))
        for z in column:
            order.append(z * xs + x)
    return order


def ring_tables(n):
    ring = snake_ring(n)
    pos = [0] * n
    for p, d in enumerate(ring):
        pos[d] = p
    return ring, pos


def ring_shift(value, ring, shift):
    n = len(ring)
    pairs = [(ring[p], ring[(p + shift) % n]) for p in range(n)]
    return lax.ppermute(value, "dp", pairs)


def ring_all_gather(shard):
    n = lax.axis_size("dp")
    ring, pos_of = ring_tables(n)
    me = lax.axis_index("dp")
    pos = jnp.asarray(pos_of, jnp.int32)[me]
    rows = shard.shape[0]
    half_steps = n // 2
    rel = [None] * n
    rel[0] = shard
    cw = shard
    ccw = shard
    for step in range(1, half_steps + 1):
        if step < half_steps:
            cw = ring_shift(cw, ring, 1)
            rel[n - step] = cw
            ccw = ring_shift(ccw, ring, -1)
            rel[step] = ccw
        else:
            first = ring_shift(cw[: rows // 2], ring, 1)
            second = ring_shift(ccw[rows // 2 :], ring, -1)
            rel[step] = jnp.concatenate([first, second], axis=0)
    stacked = jnp.stack(rel, axis=0)
    slots = (jnp.asarray(pos_of, jnp.int32) - pos) % n
    out = jnp.take(stacked, slots, axis=0)
    return out.reshape((n * rows,) + shard.shape[1:])


def ring_reduce_scatter(chunks):
    n = lax.axis_size("dp")
    ring, pos_of = ring_tables(n)
    me = lax.axis_index("dp")
    pos = jnp.asarray(pos_of, jnp.int32)[me]
    owners = jnp.asarray(ring, jnp.int32)[(pos + jnp.arange(n, dtype=jnp.int32)) % n]
    rel = jnp.take(chunks, owners, axis=0)

    def own(k):
        return rel[k % n].astype(jnp.float32)

    cw_steps = n // 2 - 1
    ccw_steps = n // 2
    cw = None
    ccw = None
    for t in range(ccw_steps):
        if t < cw_steps:
            k = cw_steps - t
            acc = own(k) if cw is None else cw.astype(jnp.float32) + own(k)
            cw = ring_shift(acc.astype(jnp.bfloat16), ring, 1)
        k = t - ccw_steps
        acc = own(k) if ccw is None else ccw.astype(jnp.float32) + own(k)
        ccw = ring_shift(acc.astype(jnp.bfloat16), ring, -1)
    return cw.astype(jnp.float32) + ccw.astype(jnp.float32) + own(0)


def body(inputs, weight_in, weight_out, cotangent):
    levels = lax.axis_size("block").bit_length() - 1
    n_dp = lax.axis_size("dp")
    weight_in_all = ring_all_gather(weight_in)
    weight_out_all = ring_all_gather(weight_out)
    pieces = [inputs]
    for level_bit in range(levels):
        pieces.append(swapped(inputs, "block", level_bit))
    in_stack = jnp.stack(pieces, axis=1)
    pre_act = jnp.einsum("tkc,ckh->th", in_stack, weight_in_all, preferred_element_type=jnp.float32)
    hidden = gelu_tanh(pre_act).astype(jnp.bfloat16)
    hid_pieces = [hidden]
    for level_bit in range(levels):
        hid_pieces.append(swapped(hidden, "block", level_bit))
    hid_stack = jnp.stack(hid_pieces, axis=1)
    outputs = jnp.einsum(
        "tkh,hkc->tc", hid_stack, weight_out_all, preferred_element_type=jnp.float32
    ).astype(jnp.bfloat16)
    grad_out_terms = jnp.einsum("tkh,tc->hkc", hid_stack, cotangent, preferred_element_type=jnp.float32)
    grad_out = ring_reduce_scatter(
        grad_out_terms.astype(jnp.bfloat16).reshape((n_dp, weight_out.shape[0]) + grad_out_terms.shape[1:])
    )
    back_terms = jnp.einsum(
        "tc,hkc->tkh", cotangent, weight_out_all, preferred_element_type=jnp.float32
    )
    back_round = back_terms.astype(jnp.bfloat16)
    hid_grad = rounded(back_terms[:, 0, :])
    for level_bit in range(levels):
        arrived = swapped(back_round[:, level_bit + 1, :], "block", level_bit)
        hid_grad = hid_grad + arrived.astype(jnp.float32)
    slope = jax.vjp(gelu_tanh, pre_act)[1](hid_grad)[0]
    pre_grad = slope.astype(jnp.bfloat16)
    in_terms = jnp.einsum(
        "th,ckh->tkc", pre_grad, weight_in_all, preferred_element_type=jnp.float32
    )
    in_round = in_terms.astype(jnp.bfloat16)
    in_total = rounded(in_terms[:, 0, :])
    for level_bit in range(levels):
        arrived = swapped(in_round[:, level_bit + 1, :], "block", level_bit)
        in_total = in_total + arrived.astype(jnp.float32)
    input_grad = in_total.astype(jnp.bfloat16)
    grad_in_terms = jnp.einsum("tkc,th->ckh", in_stack, pre_grad, preferred_element_type=jnp.float32)
    grad_in = ring_reduce_scatter(
        grad_in_terms.astype(jnp.bfloat16).reshape((n_dp, weight_in.shape[0]) + grad_in_terms.shape[1:])
    )
    return (outputs, input_grad, grad_in, grad_out)


def solution(mesh):
    placed = (P("dp", "block"), P("dp", None, "block"), P("dp", None, "block"), P("dp", "block"))
    return jax.shard_map(
        body,
        mesh=mesh,
        in_specs=placed,
        out_specs=(
            P("dp", "block"),
            P("dp", "block"),
            P("dp", None, "block"),
            P("dp", None, "block"),
        ),
        check_vma=False,
    )
```

```python
import jax
import jax.numpy as jnp
from jax import lax
from jax.sharding import PartitionSpec as P


def swapped(value, axis, distance):
    mask = 2**distance
    pairs = [(source, source ^ mask) for source in range(lax.axis_size(axis))]
    return lax.ppermute(value, axis, pairs)


def gelu_tanh(value):
    return jax.nn.gelu(value, approximate=True)


def rounded(value):
    return lax.optimization_barrier(value.astype(jnp.bfloat16)).astype(jnp.float32)


def snake_ring(n_dp):
    xs = 4 if n_dp % 4 == 0 else n_dp
    zs = n_dp // xs
    order = []
    for x in range(xs):
        column = range(zs) if x % 2 == 0 else reversed(range(zs))
        for z in column:
            order.append(z * xs + x)
    return order


def ring_tables(n):
    ring = snake_ring(n)
    pos = [0] * n
    for p, d in enumerate(ring):
        pos[d] = p
    return ring, pos


def ring_shift(value, ring, shift):
    n = len(ring)
    pairs = [(ring[p], ring[(p + shift) % n]) for p in range(n)]
    return lax.ppermute(value, "dp", pairs)


def ring_all_gather(shard):
    n = lax.axis_size("dp")
    ring, pos_of = ring_tables(n)
    me = lax.axis_index("dp")
    pos = jnp.asarray(pos_of, jnp.int32)[me]
    rows = shard.shape[0]
    half_steps = n // 2
    rel = [None] * n
    rel[0] = shard
    cw = shard
    ccw = shard
    for step in range(1, half_steps + 1):
        if step < half_steps:
            cw = ring_shift(cw, ring, 1)
            rel[n - step] = cw
            ccw = ring_shift(ccw, ring, -1)
            rel[step] = ccw
        else:
            first = ring_shift(cw[: rows // 2], ring, 1)
            second = ring_shift(ccw[rows // 2 :], ring, -1)
            rel[step] = jnp.concatenate([first, second], axis=0)
    stacked = jnp.stack(rel, axis=0)
    slots = (jnp.asarray(pos_of, jnp.int32) - pos) % n
    out = jnp.take(stacked, slots, axis=0, mode="clip")
    return out.reshape((n * rows,) + shard.shape[1:])


def ring_reduce_scatter(chunks):
    n = lax.axis_size("dp")
    ring, pos_of = ring_tables(n)
    me = lax.axis_index("dp")
    pos = jnp.asarray(pos_of, jnp.int32)[me]
    owners = jnp.asarray(ring, jnp.int32)[(pos + jnp.arange(n, dtype=jnp.int32)) % n]
    rel = jnp.take(chunks, owners, axis=0, mode="clip")

    def own(k):
        return rel[k % n].astype(jnp.float32)

    cw_steps = n // 2 - 1
    ccw_steps = n // 2
    cw = None
    ccw = None
    for t in range(ccw_steps):
        if t < cw_steps:
            k = cw_steps - t
            acc = own(k) if cw is None else cw.astype(jnp.float32) + own(k)
            cw = ring_shift(acc.astype(jnp.bfloat16), ring, 1)
        k = t - ccw_steps
        acc = own(k) if ccw is None else ccw.astype(jnp.float32) + own(k)
        ccw = ring_shift(acc.astype(jnp.bfloat16), ring, -1)
    return cw.astype(jnp.float32) + ccw.astype(jnp.float32) + own(0)


def body(inputs, weight_in, weight_out, cotangent):
    levels = lax.axis_size("block").bit_length() - 1
    n_dp = lax.axis_size("dp")
    weight_in_all = ring_all_gather(weight_in)
    weight_in_all, weight_out = lax.optimization_barrier((weight_in_all, weight_out))
    weight_out_all = ring_all_gather(weight_out)
    pieces = [inputs]
    for level_bit in range(levels):
        pieces.append(swapped(inputs, "block", level_bit))
    in_stack = jnp.stack(pieces, axis=1)
    pre_act = jnp.einsum("tkc,ckh->th", in_stack, weight_in_all, preferred_element_type=jnp.float32)
    hidden = gelu_tanh(pre_act).astype(jnp.bfloat16)
    hid_pieces = [hidden]
    for level_bit in range(levels):
        hid_pieces.append(swapped(hidden, "block", level_bit))
    hid_stack = jnp.stack(hid_pieces, axis=1)
    outputs = jnp.einsum(
        "tkh,hkc->tc", hid_stack, weight_out_all, preferred_element_type=jnp.float32
    ).astype(jnp.bfloat16)
    grad_out_terms = jnp.einsum("tkh,tc->hkc", hid_stack, cotangent, preferred_element_type=jnp.float32)
    grad_out = ring_reduce_scatter(
        grad_out_terms.astype(jnp.bfloat16).reshape((n_dp, weight_out.shape[0]) + grad_out_terms.shape[1:])
    )
    back_terms = jnp.einsum(
        "tc,hkc->tkh", cotangent, weight_out_all, preferred_element_type=jnp.float32
    )
    back_round = back_terms.astype(jnp.bfloat16)
    hid_grad = rounded(back_terms[:, 0, :])
    for level_bit in range(levels):
        arrived = swapped(back_round[:, level_bit + 1, :], "block", level_bit)
        hid_grad = hid_grad + arrived.astype(jnp.float32)
    slope = jax.vjp(gelu_tanh, pre_act)[1](hid_grad)[0]
    pre_grad = slope.astype(jnp.bfloat16)
    in_terms = jnp.einsum(
        "th,ckh->tkc", pre_grad, weight_in_all, preferred_element_type=jnp.float32
    )
    in_round = in_terms.astype(jnp.bfloat16)
    in_total = rounded(in_terms[:, 0, :])
    for level_bit in range(levels):
        arrived = swapped(in_round[:, level_bit + 1, :], "block", level_bit)
        in_total = in_total + arrived.astype(jnp.float32)
    input_grad = in_total.astype(jnp.bfloat16)
    grad_in_terms = jnp.einsum("tkc,th->ckh", in_stack, pre_grad, preferred_element_type=jnp.float32)
    grad_in = ring_reduce_scatter(
        grad_in_terms.astype(jnp.bfloat16).reshape((n_dp, weight_in.shape[0]) + grad_in_terms.shape[1:])
    )
    return (outputs, input_grad, grad_in, grad_out)


def solution(mesh):
    placed = (P("dp", "block"), P("dp", None, "block"), P("dp", None, "block"), P("dp", "block"))
    return jax.shard_map(
        body,
        mesh=mesh,
        in_specs=placed,
        out_specs=(
            P("dp", "block"),
            P("dp", "block"),
            P("dp", None, "block"),
            P("dp", None, "block"),
        ),
        check_vma=False,
    )
```

```python
import jax
import jax.numpy as jnp
from jax import lax
from jax.sharding import PartitionSpec as P


def swapped(value, axis, distance):
    mask = 2**distance
    pairs = [(source, source ^ mask) for source in range(lax.axis_size(axis))]
    return lax.ppermute(value, axis, pairs)


def gelu_tanh(value):
    return jax.nn.gelu(value, approximate=True)


def rounded(value):
    return lax.optimization_barrier(value.astype(jnp.bfloat16)).astype(jnp.float32)


def snake_ring(n_dp):
    xs = 4 if n_dp % 4 == 0 else n_dp
    zs = n_dp // xs
    order = []
    for x in range(xs):
        column = range(zs) if x % 2 == 0 else reversed(range(zs))
        for z in column:
            order.append(z * xs + x)
    return order


def ring_tables(n):
    ring = snake_ring(n)
    pos = [0] * n
    for p, d in enumerate(ring):
        pos[d] = p
    return ring, pos


def ring_shift(value, ring, shift):
    n = len(ring)
    pairs = [(ring[p], ring[(p + shift) % n]) for p in range(n)]
    return lax.ppermute(value, "dp", pairs)


def ring_all_gather(shard):
    n = lax.axis_size("dp")
    ring, pos_of = ring_tables(n)
    me = lax.axis_index("dp")
    pos = jnp.asarray(pos_of, jnp.int32)[me]
    rows = shard.shape[0]
    half_steps = n // 2
    rel = [None] * n
    rel[0] = shard
    cw = shard
    ccw = shard
    for step in range(1, half_steps + 1):
        if step < half_steps:
            cw = ring_shift(cw, ring, 1)
            rel[n - step] = cw
            ccw = ring_shift(ccw, ring, -1)
            rel[step] = ccw
        else:
            first = ring_shift(cw[: rows // 2], ring, 1)
            second = ring_shift(ccw[rows // 2 :], ring, -1)
            rel[step] = jnp.concatenate([first, second], axis=0)
    stacked = jnp.stack(rel, axis=0)
    slots = (jnp.asarray(pos_of, jnp.int32) - pos) % n
    out = jnp.take(stacked, slots, axis=0, mode="clip")
    return out.reshape((n * rows,) + shard.shape[1:])


def ring_reduce_scatter(chunks):
    n = lax.axis_size("dp")
    ring, pos_of = ring_tables(n)
    me = lax.axis_index("dp")
    pos = jnp.asarray(pos_of, jnp.int32)[me]
    owners = jnp.asarray(ring, jnp.int32)[(pos + jnp.arange(n, dtype=jnp.int32)) % n]
    rel = jnp.take(chunks, owners, axis=0, mode="clip")

    def own(k):
        return rel[k % n].astype(jnp.float32)

    cw_steps = n // 2 - 1
    ccw_steps = n // 2
    cw = None
    ccw = None
    for t in range(ccw_steps):
        if t < cw_steps:
            k = cw_steps - t
            acc = own(k) if cw is None else cw.astype(jnp.float32) + own(k)
            cw = ring_shift(acc.astype(jnp.bfloat16), ring, 1)
        k = t - ccw_steps
        acc = own(k) if ccw is None else ccw.astype(jnp.float32) + own(k)
        ccw = ring_shift(acc.astype(jnp.bfloat16), ring, -1)
    return cw.astype(jnp.float32) + ccw.astype(jnp.float32) + own(0)


def body(inputs, weight_in, weight_out, cotangent):
    levels = lax.axis_size("block").bit_length() - 1
    n_dp = lax.axis_size("dp")
    n_lv = levels + 1
    rows_in = weight_in.shape[0]
    rows_out = weight_out.shape[0]
    width_in = weight_in.shape[2]
    width_out = weight_out.shape[2]
    w_in = jnp.transpose(weight_in, (1, 0, 2))
    w_out = jnp.transpose(weight_out, (1, 0, 2)).reshape(n_lv, rows_in, width_in)
    gathered = ring_all_gather(jnp.concatenate([w_in, w_out], axis=0)).reshape(
        (n_dp, 2 * n_lv, rows_in, width_in)
    )
    weight_in_all = gathered[:, :n_lv]
    weight_out_all = gathered[:, n_lv:].reshape(n_dp, n_lv, rows_out, width_out)
    pieces = [inputs]
    for level_bit in range(levels):
        pieces.append(swapped(inputs, "block", level_bit))
    in_stack = jnp.stack(pieces, axis=1)
    tokens = inputs.shape[0]
    in_split = in_stack.reshape(tokens, n_lv, n_dp, rows_in)
    pre_act = jnp.einsum("tkjc,jkch->th", in_split, weight_in_all, preferred_element_type=jnp.float32)
    hidden = gelu_tanh(pre_act).astype(jnp.bfloat16)
    hid_pieces = [hidden]
    for level_bit in range(levels):
        hid_pieces.append(swapped(hidden, "block", level_bit))
    hid_stack = jnp.stack(hid_pieces, axis=1)
    hid_split = hid_stack.reshape(tokens, n_lv, n_dp, rows_out)
    outputs = jnp.einsum(
        "tkjh,jkhc->tc", hid_split, weight_out_all, preferred_element_type=jnp.float32
    ).astype(jnp.bfloat16)
    grad_out_terms = jnp.einsum("tkjh,tc->jkhc", hid_split, cotangent, preferred_element_type=jnp.float32)
    back_terms = jnp.einsum(
        "tc,jkhc->tkjh", cotangent, weight_out_all, preferred_element_type=jnp.float32
    ).reshape(tokens, n_lv, n_dp * rows_out)
    back_round = back_terms.astype(jnp.bfloat16)
    hid_grad = rounded(back_terms[:, 0, :])
    for level_bit in range(levels):
        arrived = swapped(back_round[:, level_bit + 1, :], "block", level_bit)
        hid_grad = hid_grad + arrived.astype(jnp.float32)
    slope = jax.vjp(gelu_tanh, pre_act)[1](hid_grad)[0]
    pre_grad = slope.astype(jnp.bfloat16)
    in_terms = jnp.einsum(
        "th,jkch->tkjc", pre_grad, weight_in_all, preferred_element_type=jnp.float32
    ).reshape(tokens, n_lv, n_dp * rows_in)
    in_round = in_terms.astype(jnp.bfloat16)
    in_total = rounded(in_terms[:, 0, :])
    for level_bit in range(levels):
        arrived = swapped(in_round[:, level_bit + 1, :], "block", level_bit)
        in_total = in_total + arrived.astype(jnp.float32)
    input_grad = in_total.astype(jnp.bfloat16)
    grad_in_terms = jnp.einsum("tkjc,th->jkch", in_split, pre_grad, preferred_element_type=jnp.float32)
    chunks = jnp.concatenate(
        [
            grad_in_terms.astype(jnp.bfloat16),
            grad_out_terms.astype(jnp.bfloat16).reshape(n_dp, n_lv, rows_in, width_in),
        ],
        axis=1,
    )
    summed = ring_reduce_scatter(chunks)
    grad_in = jnp.transpose(summed[:n_lv], (1, 0, 2))
    grad_out = jnp.transpose(summed[n_lv:].reshape(n_lv, rows_out, width_out), (1, 0, 2))
    return (outputs, input_grad, grad_in, grad_out)


def solution(mesh):
    placed = (P("dp", "block"), P("dp", None, "block"), P("dp", None, "block"), P("dp", "block"))
    return jax.shard_map(
        body,
        mesh=mesh,
        in_specs=placed,
        out_specs=(
            P("dp", "block"),
            P("dp", "block"),
            P("dp", None, "block"),
            P("dp", None, "block"),
        ),
        check_vma=False,
    )
```

```python
import jax
import jax.numpy as jnp
from jax import lax
from jax.sharding import PartitionSpec as P


def swapped(value, axis, distance):
    mask = 2**distance
    pairs = [(source, source ^ mask) for source in range(lax.axis_size(axis))]
    return lax.ppermute(value, axis, pairs)


def gelu_tanh(value):
    return jax.nn.gelu(value, approximate=True)


def rounded(value):
    return lax.optimization_barrier(value.astype(jnp.bfloat16)).astype(jnp.float32)


def snake_ring(n_dp):
    xs = 4 if n_dp % 4 == 0 else n_dp
    zs = n_dp // xs
    order = []
    for x in range(xs):
        column = range(zs) if x % 2 == 0 else reversed(range(zs))
        for z in column:
            order.append(z * xs + x)
    return order


def ring_tables(n):
    ring = snake_ring(n)
    pos = [0] * n
    for p, d in enumerate(ring):
        pos[d] = p
    return ring, pos


def ring_shift(value, ring, shift):
    n = len(ring)
    pairs = [(ring[p], ring[(p + shift) % n]) for p in range(n)]
    return lax.ppermute(value, "dp", pairs)


def ring_all_gather(shard):
    n = lax.axis_size("dp")
    ring, pos_of = ring_tables(n)
    me = lax.axis_index("dp")
    pos = jnp.asarray(pos_of, jnp.int32)[me]
    rows = shard.shape[0]
    half_steps = n // 2
    rel = [None] * n
    rel[0] = shard
    cw = shard
    ccw = shard
    for step in range(1, half_steps + 1):
        if step < half_steps:
            cw = ring_shift(cw, ring, 1)
            rel[n - step] = cw
            ccw = ring_shift(ccw, ring, -1)
            rel[step] = ccw
        else:
            first = ring_shift(cw[: rows // 2], ring, 1)
            second = ring_shift(ccw[rows // 2 :], ring, -1)
            rel[step] = jnp.concatenate([first, second], axis=0)
    stacked = jnp.stack(rel, axis=0)
    slots = (jnp.asarray(pos_of, jnp.int32) - pos) % n
    out = jnp.take(stacked, slots, axis=0, mode="clip")
    return out.reshape((n * rows,) + shard.shape[1:])


def ring_reduce_scatter(chunks):
    n = lax.axis_size("dp")
    ring, pos_of = ring_tables(n)
    me = lax.axis_index("dp")
    pos = jnp.asarray(pos_of, jnp.int32)[me]
    owners = jnp.asarray(ring, jnp.int32)[(pos + jnp.arange(n, dtype=jnp.int32)) % n]
    rel = jnp.take(chunks, owners, axis=0, mode="clip")

    def own(k):
        return rel[k % n].astype(jnp.float32)

    cw_steps = n // 2 - 1
    ccw_steps = n // 2
    cw = None
    ccw = None
    for t in range(ccw_steps):
        if t < cw_steps:
            k = cw_steps - t
            acc = own(k) if cw is None else cw.astype(jnp.float32) + own(k)
            cw = ring_shift(acc.astype(jnp.bfloat16), ring, 1)
        k = t - ccw_steps
        acc = own(k) if ccw is None else ccw.astype(jnp.float32) + own(k)
        ccw = ring_shift(acc.astype(jnp.bfloat16), ring, -1)
    return cw.astype(jnp.float32) + ccw.astype(jnp.float32) + own(0)


def body(inputs, weight_in, weight_out, cotangent):
    levels = lax.axis_size("block").bit_length() - 1
    n_dp = lax.axis_size("dp")
    weight_in_all = ring_all_gather(weight_in)
    weight_out_all = lax.all_gather(weight_out, "dp", axis=0, tiled=True)
    pieces = [inputs]
    for level_bit in range(levels):
        pieces.append(swapped(inputs, "block", level_bit))
    in_stack = jnp.stack(pieces, axis=1)
    pre_act = jnp.einsum("tkc,ckh->th", in_stack, weight_in_all, preferred_element_type=jnp.float32)
    hidden = gelu_tanh(pre_act).astype(jnp.bfloat16)
    hid_pieces = [hidden]
    for level_bit in range(levels):
        hid_pieces.append(swapped(hidden, "block", level_bit))
    hid_stack = jnp.stack(hid_pieces, axis=1)
    outputs = jnp.einsum(
        "tkh,hkc->tc", hid_stack, weight_out_all, preferred_element_type=jnp.float32
    ).astype(jnp.bfloat16)
    grad_out_terms = jnp.einsum("tkh,tc->hkc", hid_stack, cotangent, preferred_element_type=jnp.float32)
    grad_out = lax.psum_scatter(
        grad_out_terms.astype(jnp.bfloat16), "dp", scatter_dimension=0, tiled=True
    ).astype(jnp.float32)
    back_terms = jnp.einsum(
        "tc,hkc->tkh", cotangent, weight_out_all, preferred_element_type=jnp.float32
    )
    back_round = back_terms.astype(jnp.bfloat16)
    hid_grad = rounded(back_terms[:, 0, :])
    for level_bit in range(levels):
        arrived = swapped(back_round[:, level_bit + 1, :], "block", level_bit)
        hid_grad = hid_grad + arrived.astype(jnp.float32)
    slope = jax.vjp(gelu_tanh, pre_act)[1](hid_grad)[0]
    pre_grad = slope.astype(jnp.bfloat16)
    in_terms = jnp.einsum(
        "th,ckh->tkc", pre_grad, weight_in_all, preferred_element_type=jnp.float32
    )
    in_round = in_terms.astype(jnp.bfloat16)
    in_total = rounded(in_terms[:, 0, :])
    for level_bit in range(levels):
        arrived = swapped(in_round[:, level_bit + 1, :], "block", level_bit)
        in_total = in_total + arrived.astype(jnp.float32)
    input_grad = in_total.astype(jnp.bfloat16)
    grad_in_terms = jnp.einsum("tkc,th->ckh", in_stack, pre_grad, preferred_element_type=jnp.float32)
    grad_in = ring_reduce_scatter(
        grad_in_terms.astype(jnp.bfloat16).reshape((n_dp, weight_in.shape[0]) + grad_in_terms.shape[1:])
    )
    return (outputs, input_grad, grad_in, grad_out)


def solution(mesh):
    placed = (P("dp", "block"), P("dp", None, "block"), P("dp", None, "block"), P("dp", "block"))
    return jax.shard_map(
        body,
        mesh=mesh,
        in_specs=placed,
        out_specs=(
            P("dp", "block"),
            P("dp", "block"),
            P("dp", None, "block"),
            P("dp", None, "block"),
        ),
        check_vma=False,
    )
```

```python
import jax
import jax.numpy as jnp
from jax import lax
from jax.sharding import PartitionSpec as P


def swapped(value, axis, distance):
    mask = 2**distance
    pairs = [(source, source ^ mask) for source in range(lax.axis_size(axis))]
    return lax.ppermute(value, axis, pairs)


def gelu_tanh(value):
    return jax.nn.gelu(value, approximate=True)


def rounded(value):
    return lax.optimization_barrier(value.astype(jnp.bfloat16)).astype(jnp.float32)


def snake_ring(n_dp):
    xs = 4 if n_dp % 4 == 0 else n_dp
    zs = n_dp // xs
    order = []
    for x in range(xs):
        column = range(zs) if x % 2 == 0 else reversed(range(zs))
        for z in column:
            order.append(z * xs + x)
    return order


def ring_tables(n):
    ring = snake_ring(n)
    pos = [0] * n
    for p, d in enumerate(ring):
        pos[d] = p
    return ring, pos


def ring_shift(value, ring, shift):
    n = len(ring)
    pairs = [(ring[p], ring[(p + shift) % n]) for p in range(n)]
    return lax.ppermute(value, "dp", pairs)


def ring_all_gather(shard):
    n = lax.axis_size("dp")
    ring, pos_of = ring_tables(n)
    me = lax.axis_index("dp")
    pos = jnp.asarray(pos_of, jnp.int32)[me]
    rows = shard.shape[0]
    half_steps = n // 2
    rel = [None] * n
    rel[0] = shard
    cw = shard
    ccw = shard
    for step in range(1, half_steps + 1):
        if step < half_steps:
            cw = ring_shift(cw, ring, 1)
            rel[n - step] = cw
            ccw = ring_shift(ccw, ring, -1)
            rel[step] = ccw
        else:
            first = ring_shift(cw[: rows // 2], ring, 1)
            second = ring_shift(ccw[rows // 2 :], ring, -1)
            rel[step] = jnp.concatenate([first, second], axis=0)
    stacked = jnp.stack(rel, axis=0)
    slots = (jnp.asarray(pos_of, jnp.int32) - pos) % n
    out = jnp.take(stacked, slots, axis=0, mode="clip")
    return out.reshape((n * rows,) + shard.shape[1:])


def ring_reduce_scatter(chunks):
    n = lax.axis_size("dp")
    ring, pos_of = ring_tables(n)
    me = lax.axis_index("dp")
    pos = jnp.asarray(pos_of, jnp.int32)[me]
    owners = jnp.asarray(ring, jnp.int32)[(pos + jnp.arange(n, dtype=jnp.int32)) % n]
    rel = jnp.take(chunks, owners, axis=0, mode="clip")

    def own(k):
        return rel[k % n].astype(jnp.float32)

    cw_steps = n // 2 - 1
    ccw_steps = n // 2
    cw = None
    ccw = None
    for t in range(ccw_steps):
        if t < cw_steps:
            k = cw_steps - t
            acc = own(k) if cw is None else cw.astype(jnp.float32) + own(k)
            cw = ring_shift(acc.astype(jnp.bfloat16), ring, 1)
        k = t - ccw_steps
        acc = own(k) if ccw is None else ccw.astype(jnp.float32) + own(k)
        ccw = ring_shift(acc.astype(jnp.bfloat16), ring, -1)
    return cw.astype(jnp.float32) + ccw.astype(jnp.float32) + own(0)


def body(inputs, weight_in, weight_out, cotangent):
    levels = lax.axis_size("block").bit_length() - 1
    n_dp = lax.axis_size("dp")
    weight_in_all = ring_all_gather(weight_in)
    weight_out_all = ring_all_gather(weight_out)
    pieces = [inputs]
    for level_bit in range(levels):
        pieces.append(swapped(inputs, "block", level_bit))
    in_stack = jnp.stack(pieces, axis=1)
    pre_act = jnp.einsum("tkc,ckh->th", in_stack, weight_in_all, preferred_element_type=jnp.float32)
    hidden = gelu_tanh(pre_act).astype(jnp.bfloat16)
    hid_pieces = [hidden]
    for level_bit in range(levels):
        hid_pieces.append(swapped(hidden, "block", level_bit))
    hid_stack = jnp.stack(hid_pieces, axis=1)
    outputs = jnp.einsum(
        "tkh,hkc->tc", hid_stack, weight_out_all, preferred_element_type=jnp.float32
    ).astype(jnp.bfloat16)
    grad_out_terms = jnp.einsum("tkh,tc->hkc", hid_stack, cotangent, preferred_element_type=jnp.float32)
    grad_out = ring_reduce_scatter(
        grad_out_terms.astype(jnp.bfloat16).reshape((n_dp, weight_out.shape[0]) + grad_out_terms.shape[1:])
    )
    back_terms = jnp.einsum(
        "tc,hkc->tkh", cotangent, weight_out_all, preferred_element_type=jnp.float32
    )
    back_round = back_terms.astype(jnp.bfloat16)
    hid_grad = rounded(back_terms[:, 0, :])
    for level_bit in range(levels):
        arrived = swapped(back_round[:, level_bit + 1, :], "block", level_bit)
        hid_grad = hid_grad + arrived.astype(jnp.float32)
    slope = jax.vjp(gelu_tanh, pre_act)[1](hid_grad)[0]
    pre_grad = slope.astype(jnp.bfloat16)
    in_terms = jnp.einsum(
        "th,ckh->tkc", pre_grad, weight_in_all, preferred_element_type=jnp.float32
    )
    in_round = in_terms.astype(jnp.bfloat16)
    in_total = rounded(in_terms[:, 0, :])
    for level_bit in range(levels):
        arrived = swapped(in_round[:, level_bit + 1, :], "block", level_bit)
        in_total = in_total + arrived.astype(jnp.float32)
    input_grad = in_total.astype(jnp.bfloat16)
    grad_in_terms = jnp.einsum("tkc,th->ckh", in_stack, pre_grad, preferred_element_type=jnp.float32)
    grad_in = ring_reduce_scatter(
        grad_in_terms.astype(jnp.bfloat16).reshape((n_dp, weight_in.shape[0]) + grad_in_terms.shape[1:])
    )
    return (outputs, input_grad, grad_in, grad_out)


def solution(mesh):
    placed = (P("dp", "block"), P("dp", None, "block"), P("dp", None, "block"), P("dp", "block"))
    return jax.shard_map(
        body,
        mesh=mesh,
        in_specs=placed,
        out_specs=(
            P("dp", "block"),
            P("dp", "block"),
            P("dp", None, "block"),
            P("dp", None, "block"),
        ),
        check_vma=False,
    )
```

```python
import jax
import jax.numpy as jnp
from jax import lax
from jax.sharding import PartitionSpec as P


def swapped(value, axis, distance):
    mask = 2**distance
    pairs = [(source, source ^ mask) for source in range(lax.axis_size(axis))]
    return lax.ppermute(value, axis, pairs)


def gelu_tanh(value):
    return jax.nn.gelu(value, approximate=True)


def rounded(value):
    return lax.optimization_barrier(value.astype(jnp.bfloat16)).astype(jnp.float32)


def snake_ring(n_dp):
    xs = 4 if n_dp % 4 == 0 else n_dp
    zs = n_dp // xs
    order = []
    for x in range(xs):
        column = range(zs) if x % 2 == 0 else reversed(range(zs))
        for z in column:
            order.append(z * xs + x)
    return order


def ring_tables(n):
    ring = snake_ring(n)
    pos = [0] * n
    for p, d in enumerate(ring):
        pos[d] = p
    return ring, pos


def ring_shift(value, ring, shift):
    n = len(ring)
    pairs = [(ring[p], ring[(p + shift) % n]) for p in range(n)]
    return lax.ppermute(value, "dp", pairs)


def ring_all_gather(shard):
    n = lax.axis_size("dp")
    ring, pos_of = ring_tables(n)
    me = lax.axis_index("dp")
    pos = jnp.asarray(pos_of, jnp.int32)[me]
    rows = shard.shape[0]
    half_steps = n // 2
    rel = [None] * n
    rel[0] = shard
    cw = shard
    ccw = shard
    for step in range(1, half_steps + 1):
        if step < half_steps:
            cw = ring_shift(cw, ring, 1)
            rel[n - step] = cw
            ccw = ring_shift(ccw, ring, -1)
            rel[step] = ccw
        else:
            first = ring_shift(cw[: rows // 2], ring, 1)
            second = ring_shift(ccw[rows // 2 :], ring, -1)
            rel[step] = jnp.concatenate([first, second], axis=0)
    stacked = jnp.stack(rel, axis=0)
    slots = (jnp.asarray(pos_of, jnp.int32) - pos) % n
    out = jnp.take(stacked, slots, axis=0, mode="clip")
    return out.reshape((n * rows,) + shard.shape[1:])


def ring_reduce_scatter(chunks, ties=()):
    n = lax.axis_size("dp")
    ring, pos_of = ring_tables(n)
    me = lax.axis_index("dp")
    pos = jnp.asarray(pos_of, jnp.int32)[me]
    owners = jnp.asarray(ring, jnp.int32)[(pos + jnp.arange(n, dtype=jnp.int32)) % n]
    rel = jnp.take(chunks, owners, axis=0, mode="clip")

    def own(k):
        return rel[k % n].astype(jnp.float32)

    cw_steps = n // 2 - 1
    ccw_steps = n // 2
    state = {"cw": None, "ccw": None}
    tie_at = dict(ties)

    def barrier(value):
        cw, ccw, value = lax.optimization_barrier((state["cw"], state["ccw"], value))
        state["cw"], state["ccw"] = cw, ccw
        return value

    for t in range(ccw_steps):
        if t in tie_at:
            tie_at[t](barrier)
        if t < cw_steps:
            k = cw_steps - t
            cw = state["cw"]
            acc = own(k) if cw is None else cw.astype(jnp.float32) + own(k)
            state["cw"] = ring_shift(acc.astype(jnp.bfloat16), ring, 1)
        k = t - ccw_steps
        ccw = state["ccw"]
        acc = own(k) if ccw is None else ccw.astype(jnp.float32) + own(k)
        state["ccw"] = ring_shift(acc.astype(jnp.bfloat16), ring, -1)
    return state["cw"].astype(jnp.float32) + state["ccw"].astype(jnp.float32) + own(0)


def body(inputs, weight_in, weight_out, cotangent):
    levels = lax.axis_size("block").bit_length() - 1
    n_dp = lax.axis_size("dp")
    weight_in_all = ring_all_gather(weight_in)
    weight_out_all = ring_all_gather(weight_out)
    pieces = [inputs]
    for level_bit in range(levels):
        pieces.append(swapped(inputs, "block", level_bit))
    in_stack = jnp.stack(pieces, axis=1)
    pre_act = jnp.einsum("tkc,ckh->th", in_stack, weight_in_all, preferred_element_type=jnp.float32)
    hidden = gelu_tanh(pre_act).astype(jnp.bfloat16)
    hid_pieces = [hidden]
    for level_bit in range(levels):
        hid_pieces.append(swapped(hidden, "block", level_bit))
    hid_stack = jnp.stack(hid_pieces, axis=1)
    outputs = jnp.einsum(
        "tkh,hkc->tc", hid_stack, weight_out_all, preferred_element_type=jnp.float32
    ).astype(jnp.bfloat16)
    grad_out_terms = jnp.einsum("tkh,tc->hkc", hid_stack, cotangent, preferred_element_type=jnp.float32)
    back_terms = jnp.einsum(
        "tc,hkc->tkh", cotangent, weight_out_all, preferred_element_type=jnp.float32
    )
    back_round = back_terms.astype(jnp.bfloat16)
    first_term = rounded(back_terms[:, 0, :])
    held = {}

    def backward_swaps(barrier):
        arriving = barrier(back_round)
        hid_grad = first_term
        for level_bit in range(levels):
            arrived = swapped(arriving[:, level_bit + 1, :], "block", level_bit)
            hid_grad = hid_grad + arrived.astype(jnp.float32)
        slope = jax.vjp(gelu_tanh, pre_act)[1](hid_grad)[0]
        held["pre_grad"] = slope.astype(jnp.bfloat16)

    def backward_terms(barrier):
        held["pre_grad"] = barrier(held["pre_grad"])

    grad_out = ring_reduce_scatter(
        grad_out_terms.astype(jnp.bfloat16).reshape((n_dp, weight_out.shape[0]) + grad_out_terms.shape[1:]),
        ties=((2, backward_swaps), (4, backward_terms)),
    )
    pre_grad = held["pre_grad"]
    in_terms = jnp.einsum(
        "th,ckh->tkc", pre_grad, weight_in_all, preferred_element_type=jnp.float32
    )
    in_round = in_terms.astype(jnp.bfloat16)
    in_total = rounded(in_terms[:, 0, :])
    for level_bit in range(levels):
        arrived = swapped(in_round[:, level_bit + 1, :], "block", level_bit)
        in_total = in_total + arrived.astype(jnp.float32)
    input_grad = in_total.astype(jnp.bfloat16)
    grad_in_terms = jnp.einsum("tkc,th->ckh", in_stack, pre_grad, preferred_element_type=jnp.float32)
    grad_in = ring_reduce_scatter(
        grad_in_terms.astype(jnp.bfloat16).reshape((n_dp, weight_in.shape[0]) + grad_in_terms.shape[1:])
    )
    return (outputs, input_grad, grad_in, grad_out)


def solution(mesh):
    placed = (P("dp", "block"), P("dp", None, "block"), P("dp", None, "block"), P("dp", "block"))
    return jax.shard_map(
        body,
        mesh=mesh,
        in_specs=placed,
        out_specs=(
            P("dp", "block"),
            P("dp", "block"),
            P("dp", None, "block"),
            P("dp", None, "block"),
        ),
        check_vma=False,
    )
```

```python
import jax
import jax.numpy as jnp
from jax import lax
from jax.sharding import PartitionSpec as P


def swapped(value, axis, distance):
    mask = 2**distance
    pairs = [(source, source ^ mask) for source in range(lax.axis_size(axis))]
    return lax.ppermute(value, axis, pairs)


def gelu_tanh(value):
    return jax.nn.gelu(value, approximate=True)


def rounded(value):
    return lax.optimization_barrier(value.astype(jnp.bfloat16)).astype(jnp.float32)


def snake_ring(n_dp):
    xs = 4 if n_dp % 4 == 0 else n_dp
    zs = n_dp // xs
    if zs % 2 or xs < 2:
        order = []
        for x in range(xs):
            column = range(zs) if x % 2 == 0 else reversed(range(zs))
            for z in column:
                order.append(z * xs + x)
        return order
    order = [x for x in range(xs)]
    for z in range(1, zs):
        columns = range(xs - 1, 0, -1) if z % 2 else range(1, xs)
        for x in columns:
            order.append(z * xs + x)
    for z in range(zs - 1, 0, -1):
        order.append(z * xs)
    return order


def ring_tables(n):
    ring = snake_ring(n)
    pos = [0] * n
    for p, d in enumerate(ring):
        pos[d] = p
    return ring, pos


def ring_shift(value, ring, shift):
    n = len(ring)
    pairs = [(ring[p], ring[(p + shift) % n]) for p in range(n)]
    return lax.ppermute(value, "dp", pairs)


def ring_all_gather(shard):
    n = lax.axis_size("dp")
    ring, pos_of = ring_tables(n)
    me = lax.axis_index("dp")
    pos = jnp.asarray(pos_of, jnp.int32)[me]
    rows = shard.shape[0]
    half_steps = n // 2
    rel = [None] * n
    rel[0] = shard
    cw = shard
    ccw = shard
    for step in range(1, half_steps + 1):
        if step < half_steps:
            cw = ring_shift(cw, ring, 1)
            rel[n - step] = cw
            ccw = ring_shift(ccw, ring, -1)
            rel[step] = ccw
        else:
            first = ring_shift(cw[: rows // 2], ring, 1)
            second = ring_shift(ccw[rows // 2 :], ring, -1)
            rel[step] = jnp.concatenate([first, second], axis=0)
    stacked = jnp.stack(rel, axis=0)
    slots = (jnp.asarray(pos_of, jnp.int32) - pos) % n
    out = jnp.take(stacked, slots, axis=0, mode="clip")
    return out.reshape((n * rows,) + shard.shape[1:])


def ring_reduce_scatter(chunks):
    n = lax.axis_size("dp")
    ring, pos_of = ring_tables(n)
    me = lax.axis_index("dp")
    pos = jnp.asarray(pos_of, jnp.int32)[me]
    owners = jnp.asarray(ring, jnp.int32)[(pos + jnp.arange(n, dtype=jnp.int32)) % n]
    rel = jnp.take(chunks, owners, axis=0, mode="clip")

    def own(k):
        return rel[k % n].astype(jnp.float32)

    cw_steps = n // 2 - 1
    ccw_steps = n // 2
    cw = None
    ccw = None
    for t in range(ccw_steps):
        if t < cw_steps:
            k = cw_steps - t
            acc = own(k) if cw is None else cw.astype(jnp.float32) + own(k)
            cw = ring_shift(acc.astype(jnp.bfloat16), ring, 1)
        k = t - ccw_steps
        acc = own(k) if ccw is None else ccw.astype(jnp.float32) + own(k)
        ccw = ring_shift(acc.astype(jnp.bfloat16), ring, -1)
    return cw.astype(jnp.float32) + ccw.astype(jnp.float32) + own(0)


def body(inputs, weight_in, weight_out, cotangent):
    levels = lax.axis_size("block").bit_length() - 1
    n_dp = lax.axis_size("dp")
    weight_in_all = ring_all_gather(weight_in)
    weight_out_all = ring_all_gather(weight_out)
    pieces = [inputs]
    for level_bit in range(levels):
        pieces.append(swapped(inputs, "block", level_bit))
    in_stack = jnp.stack(pieces, axis=1)
    pre_act = jnp.einsum("tkc,ckh->th", in_stack, weight_in_all, preferred_element_type=jnp.float32)
    hidden = gelu_tanh(pre_act).astype(jnp.bfloat16)
    hid_pieces = [hidden]
    for level_bit in range(levels):
        hid_pieces.append(swapped(hidden, "block", level_bit))
    hid_stack = jnp.stack(hid_pieces, axis=1)
    outputs = jnp.einsum(
        "tkh,hkc->tc", hid_stack, weight_out_all, preferred_element_type=jnp.float32
    ).astype(jnp.bfloat16)
    grad_out_terms = jnp.einsum("tkh,tc->hkc", hid_stack, cotangent, preferred_element_type=jnp.float32)
    grad_out = ring_reduce_scatter(
        grad_out_terms.astype(jnp.bfloat16).reshape((n_dp, weight_out.shape[0]) + grad_out_terms.shape[1:])
    )
    back_terms = jnp.einsum(
        "tc,hkc->tkh", cotangent, weight_out_all, preferred_element_type=jnp.float32
    )
    back_round = back_terms.astype(jnp.bfloat16)
    hid_grad = rounded(back_terms[:, 0, :])
    for level_bit in range(levels):
        arrived = swapped(back_round[:, level_bit + 1, :], "block", level_bit)
        hid_grad = hid_grad + arrived.astype(jnp.float32)
    slope = jax.vjp(gelu_tanh, pre_act)[1](hid_grad)[0]
    pre_grad = slope.astype(jnp.bfloat16)
    in_terms = jnp.einsum(
        "th,ckh->tkc", pre_grad, weight_in_all, preferred_element_type=jnp.float32
    )
    in_round = in_terms.astype(jnp.bfloat16)
    in_total = rounded(in_terms[:, 0, :])
    for level_bit in range(levels):
        arrived = swapped(in_round[:, level_bit + 1, :], "block", level_bit)
        in_total = in_total + arrived.astype(jnp.float32)
    input_grad = in_total.astype(jnp.bfloat16)
    grad_in_terms = jnp.einsum("tkc,th->ckh", in_stack, pre_grad, preferred_element_type=jnp.float32)
    grad_in = ring_reduce_scatter(
        grad_in_terms.astype(jnp.bfloat16).reshape((n_dp, weight_in.shape[0]) + grad_in_terms.shape[1:])
    )
    return (outputs, input_grad, grad_in, grad_out)


def solution(mesh):
    placed = (P("dp", "block"), P("dp", None, "block"), P("dp", None, "block"), P("dp", "block"))
    return jax.shard_map(
        body,
        mesh=mesh,
        in_specs=placed,
        out_specs=(
            P("dp", "block"),
            P("dp", "block"),
            P("dp", None, "block"),
            P("dp", None, "block"),
        ),
        check_vma=False,
    )
```
